512 devices in a mesh: depth: 16 (over x_hi, y), scan: 32 (over z, x_lo, core).
Axes of the slice: x: 4 (x_hi: 2, x_lo: 2; x = x_hi * 2 + x_lo), y: 8, z: 8, core: 2. Of those that a mesh axis runs over, the one named last changes fastest.
Arguments:
- object_slice: bfloat16 [2, 4, 512, 2048], P(None, None, 'depth', 'scan'), may hold values from -4 to 4
- probe_field: bfloat16 [2, 512, 512], replicated, may hold values from -2 to 2
- offsets: int32 [64, 2], replicated, may hold values from 0 to 1536
- assignment: int32 [64], P('scan'), may hold values from 0 to 63, each once
- intensities: float32 [64, 512, 512], P('scan', 'depth'), may hold values from 0 to 3
Outputs:
- object_grad: float32 [2, 4, 512, 2048], P(None, None, 'depth', 'scan')
- probe_grad: float32 [2, 512, 512], P(None, 'depth')
The draws below stay inside these ranges and needn't reach their ends.
Inputs may be any that keep to these rules, and one draw needn't show every extreme that they name: `offsets`: each window lies inside the object window. `assignment`: every position stands in exactly one slot; slots s * 2 to s * 2 + 1 lie on index s of scan.
All inputs are finite; a program needn't handle non-finite values.
Results may differ from the reference program's by a relative error of at most 0.0003.
Values may be sent and summed in bfloat16 or wider, within the bound.
No kernel may reach another device: no remote copies, remote signals or barrier semaphores. Data moves between devices by JAX's collectives and lax.ppermute only.
A program may use at most 64 MiB of HBM per device.

```python
import math
import jax
import jax.numpy as jnp
from jax import lax

P_SIZE = 512
S = 2048
NPOS = 64
CYC = 4


def set_ends(drawn, rng, smallest, top_value):
    longest = drawn.shape.index(max(drawn.shape))
    spots = []
    for shift in (0, 1):
        where = [jax.random.randint(jax.random.fold_in(rng, axis), (), 0, length) for axis, length in enumerate(drawn.shape)]
        where[longest] = (where[longest] + shift) % drawn.shape[longest]
        spots.append(tuple(where))
    return drawn.at[spots[0]].set(smallest).at[spots[1]].set(top_value)


def block_scale(key, extent, split, smallest, largest):
    def one(dim, blocks):
        heights = jax.random.uniform(jax.random.fold_in(jax.random.fold_in(key, 6), dim), (blocks,), jnp.float32, smallest / len(split), largest / len(split))
        return jnp.repeat(jnp.exp(heights), extent[dim] // blocks).reshape((-1,) + (1,) * (len(extent) - dim - 1))

    gain = one(*split[0])
    for cut in split[1:]:
        gain = gain * one(*cut)
    return gain


def noise(stream_key, dims, width, most, split=(), kind=jnp.bfloat16):
    factor_of = block_scale(stream_key, dims, split, -0.22, 0.18) if split else 1.0
    entries = jax.random.normal(stream_key, dims, jnp.float32) * width * factor_of
    return jnp.minimum(jnp.maximum(entries, -most), most).astype(kind)


def setup_inputs(seed: int = 0) -> dict:
    splits = jax.random.split(jax.random.key(seed), 6)
    object_slice = noise(splits[0], (2, CYC, P_SIZE, S), 1.0, 4.0, ((2, 16), (3, 32)))
    probe_field = noise(splits[1], (2, P_SIZE, P_SIZE), 0.5, 2.0)
    offsets = set_ends(jax.random.randint(splits[2], (NPOS, 2), 0, S - P_SIZE + 1), jax.random.fold_in(splits[2], 1), 0, S - P_SIZE).astype(jnp.int32)
    assignment = jax.random.permutation(splits[3], NPOS).astype(jnp.int32)
    intensities = jnp.clip(3.0 * jax.random.uniform(splits[4], (NPOS, P_SIZE, P_SIZE), jnp.float32) ** block_scale(splits[4], (NPOS, P_SIZE, P_SIZE), ((0, 32), (1, 16)), -0.2, 0.2), 0.0, 3.0)
    return dict(object_slice=object_slice, probe_field=probe_field, offsets=offsets, assignment=assignment, intensities=intensities)


fresnel_scale = 4

def dft_table(size):
    index = jnp.arange(size, dtype=jnp.int32)
    turns = index[:, None] * index[None, :] % size
    angle = 2.0 * math.pi / size * turns.astype(jnp.float32)
    norm = 1.0 / math.sqrt(size)
    return (jnp.cos(angle) * norm, -jnp.sin(angle) * norm)

def chirp_phase(index, size):
    centred = index - size // 2
    period = 2 * fresnel_scale * size
    phase = centred * centred % period
    angle = math.pi / (fresnel_scale * size) * phase.astype(jnp.float32)
    return (jnp.cos(angle), jnp.sin(angle))

def contract(form, left_side, right_side):
    return jnp.einsum(form, left_side, right_side, precision=lax.Precision.HIGHEST, preferred_element_type=jnp.float32)

def complex_mix(form, left_re, left_im, right_re, right_im):
    real_part = contract(form, left_re, right_re) - contract(form, left_im, right_im)
    imag_part = contract(form, left_re, right_im) + contract(form, left_im, right_re)
    return (real_part, imag_part)

def reference(object_slice, probe_field, offsets, assignment, intensities):
    image = object_slice.reshape(2, S, S)
    table_re, table_im = dft_table(P_SIZE)
    index = jnp.arange(P_SIZE, dtype=jnp.int32)
    row_cos, row_sin = chirp_phase(index, P_SIZE)
    chirp_re = row_cos[:, None] * row_cos[None, :] - row_sin[:, None] * row_sin[None, :]
    chirp_im = row_sin[:, None] * row_cos[None, :] + row_cos[:, None] * row_sin[None, :]
    probe_re = probe_field[0].astype(jnp.float32)
    probe_im = probe_field[1].astype(jnp.float32)

    def visit(carry, slot_index):
        grad_image, grad_probe = carry
        position = offsets[assignment[slot_index]]
        top_row = position[0].astype(jnp.int32)
        left_col = position[1].astype(jnp.int32)
        corner = (jnp.int32(0), top_row, left_col)
        window = lax.dynamic_slice(image, corner, (2, P_SIZE, P_SIZE)).astype(jnp.float32)
        obj_re, obj_im = (window[0], window[1])
        wave_re = probe_re * obj_re - probe_im * obj_im
        wave_im = probe_re * obj_im + probe_im * obj_re
        psi_re = wave_re * chirp_re - wave_im * chirp_im
        psi_im = wave_re * chirp_im + wave_im * chirp_re
        half_re, half_im = complex_mix('vk,jk->vj', table_re, table_im, psi_re, psi_im)
        far_re, far_im = complex_mix('vj,ju->vu', half_re, half_im, table_re, table_im)
        excess = far_re * far_re + far_im * far_im - intensities[slot_index]
        resid_re = excess * far_re
        resid_im = excess * far_im
        mid_re, mid_im = complex_mix('vu,uj->vj', resid_re, resid_im, table_re, -table_im)
        back_re, back_im = complex_mix('vk,vj->jk', table_re, -table_im, mid_re, mid_im)
        grad_re = back_re * chirp_re + back_im * chirp_im
        grad_im = back_im * chirp_re - back_re * chirp_im
        contrib = jnp.stack([probe_re * grad_re + probe_im * grad_im, probe_re * grad_im - probe_im * grad_re])
        current = lax.dynamic_slice(grad_image, corner, (2, P_SIZE, P_SIZE))
        grad_image = lax.dynamic_update_slice(grad_image, current + contrib, corner)
        term = jnp.stack([obj_re * grad_re + obj_im * grad_im, obj_re * grad_im - obj_im * grad_re])
        return ((grad_image, grad_probe + term), None)
    start = (jnp.zeros((2, S, S), jnp.float32), jnp.zeros((2, P_SIZE, P_SIZE), jnp.float32))
    (grad_image, grad_probe), _ = lax.scan(visit, start, jnp.arange(NPOS, dtype=jnp.int32))
    return (grad_image.reshape(2, CYC, P_SIZE, S), grad_probe * NPOS ** (-0.5))
```

```python
import math

import jax
import jax.numpy as jnp
from jax import lax
from jax.sharding import PartitionSpec as P

fresnel_scale = 4


def from_behind(block, axis, distance):
    devices = range(lax.axis_size(axis))
    route = [((i - distance) % len(devices), i) for i in devices]
    return lax.ppermute(block, axis, route)


def gather_blocks(block, axis):
    count = lax.axis_size(axis)
    spread = jnp.broadcast_to(block[None], (count,) + block.shape)
    return lax.all_to_all(spread, axis, 0, 0, tiled=True)


def sum_blocks(chunks, axis):
    return jnp.sum(lax.all_to_all(chunks, axis, 0, 0, tiled=True), 0)


def dft_table(size):
    index = jnp.arange(size, dtype=jnp.int32)
    turns = index[:, None] * index[None, :] % size
    angle = 2.0 * math.pi / size * turns.astype(jnp.float32)
    norm = 1.0 / math.sqrt(size)
    return (jnp.cos(angle) * norm, -jnp.sin(angle) * norm)


def chirp_phase(index, size):
    centred = index - size // 2
    period = 2 * fresnel_scale * size
    phase = centred * centred % period
    angle = math.pi / (fresnel_scale * size) * phase.astype(jnp.float32)
    return (jnp.cos(angle), jnp.sin(angle))


def contract(form, left_side, right_side):
    return jnp.einsum(
        form,
        left_side,
        right_side,
        precision=lax.Precision.HIGHEST,
        preferred_element_type=jnp.float32,
    )


def complex_mix(form, left_re, left_im, right_re, right_im):
    real_part = contract(form, left_re, right_re) - contract(form, left_im, right_im)
    imag_part = contract(form, left_re, right_im) + contract(form, left_im, right_re)
    return (real_part, imag_part)


def on_device(object_slice, probe_field, offsets, assignment, intensities):
    depth_count = lax.axis_size("depth")
    depth_index = lax.axis_index("depth")
    rows_dev = object_slice.shape[2]
    cycles = object_slice.shape[1]
    patch_side = probe_field.shape[2]
    pos_count = assignment.shape[0]
    total_pos = pos_count * lax.axis_size("scan")
    scan_count = lax.axis_size("scan")
    gathered = gather_blocks(object_slice, "scan")
    band_rows = jnp.moveaxis(gathered, 0, 3).reshape(
        object_slice.shape[:3] + (scan_count * object_slice.shape[3],)
    )
    full_width = band_rows.shape[3]
    flat_band = band_rows.reshape(2, cycles * rows_dev, full_width)
    position = offsets[assignment]
    top_row = position[:, 0]
    left_col = position[:, 1]
    table_re, table_im = dft_table(patch_side)
    row_ids = jnp.arange(rows_dev, dtype=jnp.int32)
    col_ids = jnp.arange(patch_side, dtype=jnp.int32)
    col_cos, col_sin = chirp_phase(col_ids, patch_side)
    zero_start = jnp.int32(0)

    def cut_tile(cycle_row, column):
        return lax.dynamic_slice(
            flat_band, (zero_start, cycle_row * rows_dev, column), (2, rows_dev, patch_side)
        )

    block_first = top_row // rows_dev
    offset_in = top_row % rows_dev
    first_block = block_first + (depth_index - block_first) % depth_count
    first_cycle = first_block // depth_count
    second_cycle = jnp.minimum(first_cycle + 1, cycles - 1)
    pair_tiles = jnp.stack(
        [jax.vmap(cut_tile)(first_cycle, left_col), jax.vmap(cut_tile)(second_cycle, left_col)], 1
    )
    levels = depth_count.bit_length() - 1
    amount = (depth_count - block_first % depth_count) % depth_count
    for level in range(levels):
        moved = from_behind(pair_tiles, "depth", 1 << level)
        taken = amount >> level & 1 == 1
        pair_tiles = jnp.where(taken[:, None, None, None, None], moved, pair_tiles)
    first_tile = pair_tiles[:, 0]
    outgoing = jnp.where(depth_index == 0, pair_tiles[:, 1], first_tile)
    following = from_behind(outgoing, "depth", depth_count - 1)
    stacked = jnp.concatenate([first_tile, following], 2)

    def take_rows(tile_pair, corner_row):
        return lax.dynamic_slice_in_dim(tile_pair, corner_row, rows_dev, 1)

    patch = jax.vmap(take_rows)(stacked, offset_in)
    patch_rows = jnp.broadcast_to(depth_index * rows_dev + row_ids[None, :], (pos_count, rows_dev))
    probe_rows = lax.dynamic_slice_in_dim(probe_field, depth_index * rows_dev, rows_dev, 1)[None]
    row_cos, row_sin = chirp_phase(patch_rows, patch_side)
    chirp_re = (
        row_cos[:, :, None] * col_cos[None, None, :] - row_sin[:, :, None] * col_sin[None, None, :]
    )
    chirp_im = (
        row_sin[:, :, None] * col_cos[None, None, :] + row_cos[:, :, None] * col_sin[None, None, :]
    )
    obj_re = patch[:, 0].astype(jnp.float32)
    obj_im = patch[:, 1].astype(jnp.float32)
    probe_re = probe_rows[:, 0].astype(jnp.float32)
    probe_im = probe_rows[:, 1].astype(jnp.float32)
    wave_re = probe_re * obj_re - probe_im * obj_im
    wave_im = probe_re * obj_im + probe_im * obj_re
    psi_re = wave_re * chirp_re - wave_im * chirp_im
    psi_im = wave_re * chirp_im + wave_im * chirp_re
    half_re, half_im = complex_mix("vk,pjk->pvj", table_re, table_im, psi_re, psi_im)
    half_re, half_im = lax.all_to_all(
        jnp.stack([half_re, half_im]), "depth", split_axis=2, concat_axis=3, tiled=True
    )
    far_re, far_im = complex_mix("pvj,ju->pvu", half_re, half_im, table_re, table_im)
    excess = far_re * far_re + far_im * far_im - intensities
    resid_re = excess * far_re
    resid_im = excess * far_im
    mid_re, mid_im = complex_mix("pvu,uj->pvj", resid_re, resid_im, table_re, -table_im)
    mid_re, mid_im = lax.all_to_all(
        jnp.stack([mid_re, mid_im]), "depth", split_axis=3, concat_axis=2, tiled=True
    )
    back_re, back_im = complex_mix("vk,pvj->pjk", table_re, -table_im, mid_re, mid_im)
    grad_re = back_re * chirp_re + back_im * chirp_im
    grad_im = back_im * chirp_re - back_re * chirp_im
    contrib = jnp.stack(
        [probe_re * grad_re + probe_im * grad_im, probe_re * grad_im - probe_im * grad_re], 1
    )
    term_re = obj_re * grad_re + obj_im * grad_im
    term_im = obj_re * grad_im - obj_im * grad_re
    grad_band = jnp.zeros((2, cycles * rows_dev, full_width), jnp.float32)

    def add_tile(band_now, tile_value, cycle_row, column):
        corner = (zero_start, cycle_row * rows_dev, column)
        current = lax.dynamic_slice(band_now, corner, (2, rows_dev, patch_side))
        return lax.dynamic_update_slice(band_now, current + tile_value, corner)

    empty_window = jnp.zeros((pos_count, 2, 2 * rows_dev, patch_side), jnp.float32)

    def place_rows(window_zero, tile_rows, corner_row):
        return lax.dynamic_update_slice_in_dim(window_zero, tile_rows, corner_row, 1)

    placed = jax.vmap(place_rows)(empty_window, contrib, offset_in)
    head_part = placed[:, :, :rows_dev]
    tail_part = placed[:, :, rows_dev:]
    returned = from_behind(tail_part, "depth", 1)
    is_first = depth_index == 0
    head_part = jnp.where(is_first, head_part, head_part + returned)
    second_part = jnp.where(is_first, returned, jnp.zeros_like(returned))
    grad_pair = jnp.stack([head_part, second_part], 1)
    amount_back = block_first % depth_count
    for level in range(levels):
        moved_back = from_behind(grad_pair, "depth", 1 << level)
        taken_back = amount_back >> level & 1 == 1
        grad_pair = jnp.where(taken_back[:, None, None, None, None], moved_back, grad_pair)
    for slot_index in range(pos_count):
        grad_band = add_tile(
            grad_band, grad_pair[slot_index, 0], first_cycle[slot_index], left_col[slot_index]
        )
        grad_band = add_tile(
            grad_band, grad_pair[slot_index, 1], second_cycle[slot_index], left_col[slot_index]
        )
    probe_sum = jnp.stack([jnp.sum(term_re, 0), jnp.sum(term_im, 0)])
    probe_part = sum_blocks(probe_sum.reshape(scan_count, -1), "scan")
    probe_grad = gather_blocks(probe_part, "scan").reshape(probe_sum.shape)
    col_chunks = grad_band.reshape(2, cycles * rows_dev, scan_count, full_width // scan_count)
    object_grad = sum_blocks(jnp.moveaxis(col_chunks, 2, 0), "scan").reshape(
        2, cycles, rows_dev, full_width // scan_count
    )
    return (object_grad, probe_grad * total_pos ** (-0.5))


def solution(mesh):
    return jax.shard_map(
        on_device,
        mesh=mesh,
        in_specs=(P(None, None, "depth", "scan"), P(), P(), P("scan"), P("scan", "depth", None)),
        out_specs=(P(None, None, "depth", "scan"), P(None, "depth", None)),
        check_vma=False,
    )
```

```python
import math

import jax
import jax.numpy as jnp
from jax import lax
from jax.sharding import PartitionSpec as P

fresnel_scale = 4


def from_behind(block, axis, distance):
    devices = range(lax.axis_size(axis))
    route = [((i - distance) % len(devices), i) for i in devices]
    return lax.ppermute(block, axis, route)


def gather_blocks(block, axis):
    count = lax.axis_size(axis)
    spread = jnp.broadcast_to(block[None], (count,) + block.shape)
    return lax.all_to_all(spread, axis, 0, 0, tiled=True)


def sum_blocks(chunks, axis):
    return jnp.sum(lax.all_to_all(chunks, axis, 0, 0, tiled=True), 0)


def dft_table(size):
    index = jnp.arange(size, dtype=jnp.int32)
    turns = index[:, None] * index[None, :] % size
    angle = 2.0 * math.pi / size * turns.astype(jnp.float32)
    norm = 1.0 / math.sqrt(size)
    return (jnp.cos(angle) * norm, -jnp.sin(angle) * norm)


def chirp_phase(index, size):
    centred = index - size // 2
    period = 2 * fresnel_scale * size
    phase = centred * centred % period
    angle = math.pi / (fresnel_scale * size) * phase.astype(jnp.float32)
    return (jnp.cos(angle), jnp.sin(angle))


def contract(form, left_side, right_side):
    return jnp.einsum(
        form,
        left_side,
        right_side,
        precision=lax.Precision.HIGHEST,
        preferred_element_type=jnp.float32,
    )


def complex_mix(form, left_re, left_im, right_re, right_im):
    real_part = contract(form, left_re, right_re) - contract(form, left_im, right_im)
    imag_part = contract(form, left_re, right_im) + contract(form, left_im, right_re)
    return (real_part, imag_part)


def on_device(object_slice, probe_field, offsets, assignment, intensities):
    depth_count = lax.axis_size("depth")
    depth_index = lax.axis_index("depth")
    scan_count = lax.axis_size("scan")
    cycles = object_slice.shape[1]
    rows_dev = object_slice.shape[2]
    patch_side = probe_field.shape[2]
    pos_count = assignment.shape[0]
    total_pos = pos_count * scan_count
    gathered = gather_blocks(object_slice, "scan")
    band = jnp.moveaxis(gathered, 0, 3).reshape(
        object_slice.shape[:3] + (scan_count * object_slice.shape[3],)
    )
    full_width = band.shape[3]
    position = offsets[assignment]
    top_row = position[:, 0]
    left_col = position[:, 1]
    table_re, table_im = dft_table(patch_side)
    twice_re = jnp.concatenate([table_re, table_re], 0)
    twice_im = jnp.concatenate([table_im, table_im], 0)
    probe_twice = jnp.concatenate([probe_field, probe_field], 1)
    row_ids = jnp.arange(rows_dev, dtype=jnp.int32)
    col_ids = jnp.arange(patch_side, dtype=jnp.int32)
    col_cos, col_sin = chirp_phase(col_ids, patch_side)
    local_rows = depth_index * rows_dev + row_ids
    shift_of = (local_rows[None, :] - top_row[:, None]) % patch_side
    cycle_of = (top_row[:, None] + shift_of) // patch_side
    obj_list, probe_list, t_re_list, t_im_list = [], [], [], []
    for slot in range(pos_count):
        chosen = band[:, 0]
        for cyc in range(1, cycles):
            chosen = jnp.where((cycle_of[slot] == cyc)[None, :, None], band[:, cyc], chosen)
        obj_list.append(lax.dynamic_slice_in_dim(chosen, left_col[slot], patch_side, 2))
        first_row = (depth_index * rows_dev - top_row[slot]) % patch_side
        probe_list.append(lax.dynamic_slice_in_dim(probe_twice, first_row, rows_dev, 1))
        table_start = (patch_side - top_row[slot] % patch_side) % patch_side
        t_re_list.append(lax.dynamic_slice_in_dim(twice_re, table_start, patch_side, 0))
        t_im_list.append(lax.dynamic_slice_in_dim(twice_im, table_start, patch_side, 0))
    patch = jnp.stack(obj_list)
    probe_rows = jnp.stack(probe_list)
    shift_re = jnp.stack(t_re_list)
    shift_im = jnp.stack(t_im_list)
    row_cos, row_sin = chirp_phase(shift_of, patch_side)
    chirp_re = (
        row_cos[:, :, None] * col_cos[None, None, :] - row_sin[:, :, None] * col_sin[None, None, :]
    )
    chirp_im = (
        row_sin[:, :, None] * col_cos[None, None, :] + row_cos[:, :, None] * col_sin[None, None, :]
    )
    obj_re = patch[:, 0].astype(jnp.float32)
    obj_im = patch[:, 1].astype(jnp.float32)
    probe_re = probe_rows[:, 0].astype(jnp.float32)
    probe_im = probe_rows[:, 1].astype(jnp.float32)
    wave_re = probe_re * obj_re - probe_im * obj_im
    wave_im = probe_re * obj_im + probe_im * obj_re
    psi_re = wave_re * chirp_re - wave_im * chirp_im
    psi_im = wave_re * chirp_im + wave_im * chirp_re
    half_re, half_im = complex_mix("vk,pjk->pvj", table_re, table_im, psi_re, psi_im)
    half_re, half_im = lax.all_to_all(
        jnp.stack([half_re, half_im]), "depth", split_axis=2, concat_axis=3, tiled=True
    )
    far_re, far_im = complex_mix("pvj,pju->pvu", half_re, half_im, shift_re, shift_im)
    excess = far_re * far_re + far_im * far_im - intensities
    resid_re = excess * far_re
    resid_im = excess * far_im
    mid_re, mid_im = complex_mix("pvu,pju->pvj", resid_re, resid_im, shift_re, -shift_im)
    mid_re, mid_im = lax.all_to_all(
        jnp.stack([mid_re, mid_im]), "depth", split_axis=3, concat_axis=2, tiled=True
    )
    back_re, back_im = complex_mix("vk,pvj->pjk", table_re, -table_im, mid_re, mid_im)
    grad_re = back_re * chirp_re + back_im * chirp_im
    grad_im = back_im * chirp_re - back_re * chirp_im
    contrib = jnp.stack(
        [probe_re * grad_re + probe_im * grad_im, probe_re * grad_im - probe_im * grad_re], 1
    )
    term = jnp.stack([obj_re * grad_re + obj_im * grad_im, obj_re * grad_im - obj_im * grad_re], 1)
    grad_band = jnp.zeros((2, cycles, rows_dev, full_width), jnp.float32)
    for slot in range(pos_count):
        placed = lax.dynamic_update_slice_in_dim(
            jnp.zeros((2, rows_dev, full_width), jnp.float32), contrib[slot], left_col[slot], 2
        )
        for cyc in range(cycles):
            taken = (cycle_of[slot] == cyc)[None, :, None]
            grad_band = grad_band.at[:, cyc].add(jnp.where(taken, placed, 0.0))
    in_block = top_row % patch_side % rows_dev
    block_shift = top_row % patch_side // rows_dev
    term_twice = jnp.concatenate([term, term], 2)
    rolled = jax.vmap(lambda t, b: lax.dynamic_slice_in_dim(t, b, rows_dev, 1))(term_twice, in_block)
    upper = (row_ids[None, :] >= rows_dev - in_block[:, None])[:, None, :, None]
    lower_part = jnp.where(upper, 0.0, rolled)
    upper_part = jnp.where(upper, rolled, 0.0)
    joined = lower_part + from_behind(upper_part, "depth", depth_count - 1)
    levels = depth_count.bit_length() - 1
    for level in range(levels):
        moved = from_behind(joined, "depth", depth_count - (1 << level))
        taken = (block_shift >> level & 1) == 1
        joined = jnp.where(taken[:, None, None, None], moved, joined)
    probe_sum = jnp.sum(joined, 0)
    probe_part = sum_blocks(probe_sum.reshape(scan_count, -1), "scan")
    probe_grad = gather_blocks(probe_part, "scan").reshape(probe_sum.shape)
    col_chunks = grad_band.reshape(2, cycles, rows_dev, scan_count, full_width // scan_count)
    object_grad = sum_blocks(jnp.moveaxis(col_chunks, 3, 0), "scan")
    return (object_grad, probe_grad * total_pos ** (-0.5))


def solution(mesh):
    return jax.shard_map(
        on_device,
        mesh=mesh,
        in_specs=(P(None, None, "depth", "scan"), P(), P(), P("scan"), P("scan", "depth", None)),
        out_specs=(P(None, None, "depth", "scan"), P(None, "depth", None)),
        check_vma=False,
    )
```

```python
import math

import jax
import jax.numpy as jnp
from jax import lax
from jax.sharding import PartitionSpec as P

fresnel_scale = 4


def from_behind(block, axis, distance):
    devices = range(lax.axis_size(axis))
    route = [((i - distance) % len(devices), i) for i in devices]
    return lax.ppermute(block, axis, route)


def gather_blocks(block, axis):
    count = lax.axis_size(axis)
    spread = jnp.broadcast_to(block[None], (count,) + block.shape)
    return lax.all_to_all(spread, axis, 0, 0, tiled=True)


def sum_blocks(chunks, axis):
    return jnp.sum(lax.all_to_all(chunks, axis, 0, 0, tiled=True), 0)


def dft_table(size):
    index = jnp.arange(size, dtype=jnp.int32)
    turns = index[:, None] * index[None, :] % size
    angle = 2.0 * math.pi / size * turns.astype(jnp.float32)
    norm = 1.0 / math.sqrt(size)
    return (jnp.cos(angle) * norm, -jnp.sin(angle) * norm)


def chirp_phase(index, size):
    centred = index - size // 2
    period = 2 * fresnel_scale * size
    phase = centred * centred % period
    angle = math.pi / (fresnel_scale * size) * phase.astype(jnp.float32)
    return (jnp.cos(angle), jnp.sin(angle))


def contract(form, left_side, right_side):
    return jnp.einsum(
        form,
        left_side,
        right_side,
        precision=lax.Precision.HIGHEST,
        preferred_element_type=jnp.float32,
    )


def complex_mix(form, left_re, left_im, right_re, right_im):
    real_part = contract(form, left_re, right_re) - contract(form, left_im, right_im)
    imag_part = contract(form, left_re, right_im) + contract(form, left_im, right_re)
    return (real_part, imag_part)


def on_device(object_slice, probe_field, offsets, assignment, intensities):
    depth_count = lax.axis_size("depth")
    depth_index = lax.axis_index("depth")
    scan_count = lax.axis_size("scan")
    cycles = object_slice.shape[1]
    rows_dev = object_slice.shape[2]
    patch_side = probe_field.shape[2]
    pos_count = assignment.shape[0]
    total_pos = pos_count * scan_count
    width = object_slice.shape[3]
    full_width = scan_count * width
    all_slots = gather_blocks(assignment, "scan").reshape(total_pos)
    every_top = offsets[all_slots, 0]
    position = offsets[assignment]
    top_row = position[:, 0]
    left_col = position[:, 1]
    table_re, table_im = dft_table(patch_side)
    twice_re = jnp.concatenate([table_re, table_re], 0)
    twice_im = jnp.concatenate([table_im, table_im], 0)
    probe_twice = jnp.concatenate([probe_field, probe_field], 1)
    row_ids = jnp.arange(rows_dev, dtype=jnp.int32)
    col_ids = jnp.arange(patch_side, dtype=jnp.int32)
    col_cos, col_sin = chirp_phase(col_ids, patch_side)
    local_rows = depth_index * rows_dev + row_ids
    every_cycle = (every_top[:, None] + (local_rows[None, :] - every_top[:, None]) % patch_side) // patch_side
    picked = jnp.broadcast_to(object_slice[:, 0][None], (total_pos,) + object_slice[:, 0].shape)
    for cyc in range(1, cycles):
        picked = jnp.where((every_cycle == cyc)[:, None, :, None], object_slice[:, cyc][None], picked)
    received = lax.all_to_all(
        picked.reshape((scan_count, pos_count) + picked.shape[1:]), "scan", 0, 0, tiled=True
    )
    band = jnp.moveaxis(received, 0, 3).reshape(pos_count, 2, rows_dev, full_width)
    shift_of = (local_rows[None, :] - top_row[:, None]) % patch_side
    cycle_of = (top_row[:, None] + shift_of) // patch_side
    obj_list, probe_list, t_re_list, t_im_list = [], [], [], []
    for slot in range(pos_count):
        obj_list.append(lax.dynamic_slice_in_dim(band[slot], left_col[slot], patch_side, 2))
        first_row = (depth_index * rows_dev - top_row[slot]) % patch_side
        probe_list.append(lax.dynamic_slice_in_dim(probe_twice, first_row, rows_dev, 1))
        table_start = (patch_side - top_row[slot] % patch_side) % patch_side
        t_re_list.append(lax.dynamic_slice_in_dim(twice_re, table_start, patch_side, 0))
        t_im_list.append(lax.dynamic_slice_in_dim(twice_im, table_start, patch_side, 0))
    patch = jnp.stack(obj_list)
    probe_rows = jnp.stack(probe_list)
    shift_re = jnp.stack(t_re_list)
    shift_im = jnp.stack(t_im_list)
    row_cos, row_sin = chirp_phase(shift_of, patch_side)
    chirp_re = (
        row_cos[:, :, None] * col_cos[None, None, :] - row_sin[:, :, None] * col_sin[None, None, :]
    )
    chirp_im = (
        row_sin[:, :, None] * col_cos[None, None, :] + row_cos[:, :, None] * col_sin[None, None, :]
    )
    obj_re = patch[:, 0].astype(jnp.float32)
    obj_im = patch[:, 1].astype(jnp.float32)
    probe_re = probe_rows[:, 0].astype(jnp.float32)
    probe_im = probe_rows[:, 1].astype(jnp.float32)
    wave_re = probe_re * obj_re - probe_im * obj_im
    wave_im = probe_re * obj_im + probe_im * obj_re
    psi_re = wave_re * chirp_re - wave_im * chirp_im
    psi_im = wave_re * chirp_im + wave_im * chirp_re
    half_re, half_im = complex_mix("vk,pjk->pvj", table_re, table_im, psi_re, psi_im)
    half_re, half_im = lax.all_to_all(
        jnp.stack([half_re, half_im]), "depth", split_axis=2, concat_axis=3, tiled=True
    )
    far_re, far_im = complex_mix("pvj,pju->pvu", half_re, half_im, shift_re, shift_im)
    excess = far_re * far_re + far_im * far_im - intensities
    resid_re = excess * far_re
    resid_im = excess * far_im
    mid_re, mid_im = complex_mix("pvu,pju->pvj", resid_re, resid_im, shift_re, -shift_im)
    mid_re, mid_im = lax.all_to_all(
        jnp.stack([mid_re, mid_im]), "depth", split_axis=3, concat_axis=2, tiled=True
    )
    back_re, back_im = complex_mix("vk,pvj->pjk", table_re, -table_im, mid_re, mid_im)
    grad_re = back_re * chirp_re + back_im * chirp_im
    grad_im = back_im * chirp_re - back_re * chirp_im
    contrib = jnp.stack(
        [probe_re * grad_re + probe_im * grad_im, probe_re * grad_im - probe_im * grad_re], 1
    )
    term = jnp.stack([obj_re * grad_re + obj_im * grad_im, obj_re * grad_im - obj_im * grad_re], 1)
    placed = jax.vmap(
        lambda tile, col: lax.dynamic_update_slice_in_dim(
            jnp.zeros((2, rows_dev, full_width), jnp.float32), tile, col, 2
        )
    )(contrib, left_col)
    grad_chunks = jnp.moveaxis(placed.reshape(pos_count, 2, rows_dev, scan_count, width), 3, 0)
    grad_back = lax.all_to_all(grad_chunks, "scan", 0, 0, tiled=True).reshape(
        (total_pos, 2, rows_dev, width)
    )
    object_grad = jnp.stack(
        [
            jnp.sum(jnp.where((every_cycle == cyc)[:, None, :, None], grad_back, 0.0), 0)
            for cyc in range(cycles)
        ],
        1,
    )
    in_block = top_row % patch_side % rows_dev
    block_shift = top_row % patch_side // rows_dev
    term_twice = jnp.concatenate([term, term], 2)
    rolled = jax.vmap(lambda t, b: lax.dynamic_slice_in_dim(t, b, rows_dev, 1))(term_twice, in_block)
    upper = (row_ids[None, :] >= rows_dev - in_block[:, None])[:, None, :, None]
    lower_part = jnp.where(upper, 0.0, rolled)
    upper_part = jnp.where(upper, rolled, 0.0)
    joined = lower_part + from_behind(upper_part, "depth", depth_count - 1)
    levels = depth_count.bit_length() - 1
    for level in range(levels):
        moved = from_behind(joined, "depth", depth_count - (1 << level))
        taken = (block_shift >> level & 1) == 1
        joined = jnp.where(taken[:, None, None, None], moved, joined)
    probe_sum = jnp.sum(joined, 0)
    probe_part = sum_blocks(probe_sum.reshape(scan_count, -1), "scan")
    probe_grad = gather_blocks(probe_part, "scan").reshape(probe_sum.shape)
    return (object_grad, probe_grad * total_pos ** (-0.5))


def solution(mesh):
    return jax.shard_map(
        on_device,
        mesh=mesh,
        in_specs=(P(None, None, "depth", "scan"), P(), P(), P("scan"), P("scan", "depth", None)),
        out_specs=(P(None, None, "depth", "scan"), P(None, "depth", None)),
        check_vma=False,
    )
```

```python
import math

import jax
import jax.numpy as jnp
from jax import lax
from jax.sharding import PartitionSpec as P

fresnel_scale = 4


def from_behind(block, axis, distance):
    devices = range(lax.axis_size(axis))
    route = [((i - distance) % len(devices), i) for i in devices]
    return lax.ppermute(block, axis, route)


def gather_blocks(block, axis):
    count = lax.axis_size(axis)
    spread = jnp.broadcast_to(block[None], (count,) + block.shape)
    return lax.all_to_all(spread, axis, 0, 0, tiled=True)


def sum_blocks(chunks, axis):
    return jnp.sum(lax.all_to_all(chunks, axis, 0, 0, tiled=True), 0)


def dft_table(size):
    index = jnp.arange(size, dtype=jnp.int32)
    turns = index[:, None] * index[None, :] % size
    angle = 2.0 * math.pi / size * turns.astype(jnp.float32)
    norm = 1.0 / math.sqrt(size)
    return (jnp.cos(angle) * norm, -jnp.sin(angle) * norm)


def chirp_phase(index, size):
    centred = index - size // 2
    period = 2 * fresnel_scale * size
    phase = centred * centred % period
    angle = math.pi / (fresnel_scale * size) * phase.astype(jnp.float32)
    return (jnp.cos(angle), jnp.sin(angle))


def contract(form, left_side, right_side):
    return jnp.einsum(
        form,
        left_side,
        right_side,
        precision=lax.Precision.HIGHEST,
        preferred_element_type=jnp.float32,
    )


def complex_mix(form, left_re, left_im, right_re, right_im):
    real_part = contract(form, left_re, right_re) - contract(form, left_im, right_im)
    imag_part = contract(form, left_re, right_im) + contract(form, left_im, right_re)
    return (real_part, imag_part)


def on_device(object_slice, probe_field, offsets, assignment, intensities):
    depth_count = lax.axis_size("depth")
    depth_index = lax.axis_index("depth")
    scan_count = lax.axis_size("scan")
    cycles = object_slice.shape[1]
    rows_dev = object_slice.shape[2]
    patch_side = probe_field.shape[2]
    pos_count = assignment.shape[0]
    total_pos = pos_count * scan_count
    width = object_slice.shape[3]
    full_width = scan_count * width
    all_slots = gather_blocks(assignment, "scan").reshape(total_pos)
    every_top = offsets[all_slots, 0]
    position = offsets[assignment]
    top_row = position[:, 0]
    left_col = position[:, 1]
    table_re, table_im = dft_table(patch_side)
    twice_re = jnp.concatenate([table_re, table_re], 0)
    twice_im = jnp.concatenate([table_im, table_im], 0)
    probe_twice = jnp.concatenate([probe_field, probe_field], 1)
    row_ids = jnp.arange(rows_dev, dtype=jnp.int32)
    col_ids = jnp.arange(patch_side, dtype=jnp.int32)
    col_cos, col_sin = chirp_phase(col_ids, patch_side)
    local_rows = depth_index * rows_dev + row_ids
    every_cycle = (every_top[:, None] + (local_rows[None, :] - every_top[:, None]) % patch_side) // patch_side
    picked = jnp.broadcast_to(object_slice[:, 0][None], (total_pos,) + object_slice[:, 0].shape)
    for cyc in range(1, cycles):
        picked = jnp.where((every_cycle == cyc)[:, None, :, None], object_slice[:, cyc][None], picked)
    received = lax.all_to_all(
        picked.reshape((scan_count, pos_count) + picked.shape[1:]), "scan", 0, 0, tiled=True
    )
    band = jnp.moveaxis(received, 0, 3).reshape(pos_count, 2, rows_dev, full_width)
    shift_of = (local_rows[None, :] - top_row[:, None]) % patch_side
    cycle_of = (top_row[:, None] + shift_of) // patch_side
    obj_list, probe_list, t_re_list, t_im_list = [], [], [], []
    for slot in range(pos_count):
        obj_list.append(lax.dynamic_slice_in_dim(band[slot], left_col[slot], patch_side, 2))
        first_row = (depth_index * rows_dev - top_row[slot]) % patch_side
        probe_list.append(lax.dynamic_slice_in_dim(probe_twice, first_row, rows_dev, 1))
        table_start = (patch_side - top_row[slot] % patch_side) % patch_side
        t_re_list.append(lax.dynamic_slice_in_dim(twice_re, table_start, patch_side, 0))
        t_im_list.append(lax.dynamic_slice_in_dim(twice_im, table_start, patch_side, 0))
    patch = jnp.stack(obj_list)
    in_block = top_row % patch_side % rows_dev
    block_shift = top_row % patch_side // rows_dev
    patch_twice = jnp.concatenate([patch, patch], 2)
    rolled = jax.vmap(lambda t, b: lax.dynamic_slice_in_dim(t, b, rows_dev, 1))(patch_twice, in_block)
    upper = (row_ids[None, :] >= rows_dev - in_block[:, None])[:, None, :, None]
    aligned = jnp.where(upper, from_behind(rolled, "depth", depth_count - 1), rolled)
    levels = depth_count.bit_length() - 1
    for level in range(levels):
        moved = from_behind(aligned, "depth", depth_count - (1 << level))
        taken = (block_shift >> level & 1) == 1
        aligned = jnp.where(taken[:, None, None, None], moved, aligned)
    probe_rows = jnp.stack(probe_list)
    shift_re = jnp.stack(t_re_list)
    shift_im = jnp.stack(t_im_list)
    row_cos, row_sin = chirp_phase(shift_of, patch_side)
    chirp_re = (
        row_cos[:, :, None] * col_cos[None, None, :] - row_sin[:, :, None] * col_sin[None, None, :]
    )
    chirp_im = (
        row_sin[:, :, None] * col_cos[None, None, :] + row_cos[:, :, None] * col_sin[None, None, :]
    )
    obj_re = patch[:, 0].astype(jnp.float32)
    obj_im = patch[:, 1].astype(jnp.float32)
    probe_re = probe_rows[:, 0].astype(jnp.float32)
    probe_im = probe_rows[:, 1].astype(jnp.float32)
    wave_re = probe_re * obj_re - probe_im * obj_im
    wave_im = probe_re * obj_im + probe_im * obj_re
    psi_re = wave_re * chirp_re - wave_im * chirp_im
    psi_im = wave_re * chirp_im + wave_im * chirp_re
    half_re, half_im = complex_mix("vk,pjk->pvj", table_re, table_im, psi_re, psi_im)
    half_re, half_im = lax.all_to_all(
        jnp.stack([half_re, half_im]), "depth", split_axis=2, concat_axis=3, tiled=True
    )
    far_re, far_im = complex_mix("pvj,pju->pvu", half_re, half_im, shift_re, shift_im)
    excess = far_re * far_re + far_im * far_im - intensities
    resid_re = excess * far_re
    resid_im = excess * far_im
    mid_re, mid_im = complex_mix("pvu,pju->pvj", resid_re, resid_im, shift_re, -shift_im)
    mid_pair = jnp.stack([mid_re, mid_im], 1)
    mid_pair_twice = jnp.concatenate([mid_pair, mid_pair], 3)
    mid_probe = jax.vmap(lambda t, b: lax.dynamic_slice_in_dim(t, b, patch_side, 2))(
        mid_pair_twice, top_row % patch_side
    )
    mid_all = lax.all_to_all(
        jnp.stack([mid_pair, mid_probe]), "depth", split_axis=4, concat_axis=3, tiled=True
    )
    back_re, back_im = complex_mix(
        "vk,pvj->pjk", table_re, -table_im, mid_all[0, :, 0], mid_all[0, :, 1]
    )
    pback_re, pback_im = complex_mix(
        "vk,pvj->pjk", table_re, -table_im, mid_all[1, :, 0], mid_all[1, :, 1]
    )
    prow_cos, prow_sin = chirp_phase(local_rows, patch_side)
    pchirp_re = prow_cos[:, None] * col_cos[None, :] - prow_sin[:, None] * col_sin[None, :]
    pchirp_im = prow_sin[:, None] * col_cos[None, :] + prow_cos[:, None] * col_sin[None, :]
    pgrad_re = pback_re * pchirp_re + pback_im * pchirp_im
    pgrad_im = pback_im * pchirp_re - pback_re * pchirp_im
    win_re = aligned[:, 0].astype(jnp.float32)
    win_im = aligned[:, 1].astype(jnp.float32)
    grad_re = back_re * chirp_re + back_im * chirp_im
    grad_im = back_im * chirp_re - back_re * chirp_im
    contrib = jnp.stack(
        [probe_re * grad_re + probe_im * grad_im, probe_re * grad_im - probe_im * grad_re], 1
    )
    term = jnp.stack(
        [win_re * pgrad_re + win_im * pgrad_im, win_re * pgrad_im - win_im * pgrad_re], 1
    )
    placed = jax.vmap(
        lambda tile, col: lax.dynamic_update_slice_in_dim(
            jnp.zeros((2, rows_dev, full_width), jnp.float32), tile, col, 2
        )
    )(contrib, left_col)
    grad_chunks = jnp.moveaxis(placed.reshape(pos_count, 2, rows_dev, scan_count, width), 3, 0)
    grad_back = lax.all_to_all(grad_chunks, "scan", 0, 0, tiled=True).reshape(
        (total_pos, 2, rows_dev, width)
    )
    object_grad = jnp.stack(
        [
            jnp.sum(jnp.where((every_cycle == cyc)[:, None, :, None], grad_back, 0.0), 0)
            for cyc in range(cycles)
        ],
        1,
    )
    probe_sum = jnp.sum(term, 0)
    probe_part = sum_blocks(probe_sum.reshape(scan_count, -1), "scan")
    probe_grad = gather_blocks(probe_part, "scan").reshape(probe_sum.shape)
    return (object_grad, probe_grad * total_pos ** (-0.5))


def solution(mesh):
    return jax.shard_map(
        on_device,
        mesh=mesh,
        in_specs=(P(None, None, "depth", "scan"), P(), P(), P("scan"), P("scan", "depth", None)),
        out_specs=(P(None, None, "depth", "scan"), P(None, "depth", None)),
        check_vma=False,
    )
```

```python
import math

import jax
import jax.numpy as jnp
from jax import lax
from jax.sharding import PartitionSpec as P

fresnel_scale = 4


def from_behind(block, axis, distance):
    devices = range(lax.axis_size(axis))
    route = [((i - distance) % len(devices), i) for i in devices]
    return lax.ppermute(block, axis, route)


def gather_blocks(block, axis):
    count = lax.axis_size(axis)
    spread = jnp.broadcast_to(block[None], (count,) + block.shape)
    return lax.all_to_all(spread, axis, 0, 0, tiled=True)


def sum_blocks(chunks, axis):
    return jnp.sum(lax.all_to_all(chunks, axis, 0, 0, tiled=True), 0)


def dft_table(size):
    index = jnp.arange(size, dtype=jnp.int32)
    turns = index[:, None] * index[None, :] % size
    angle = 2.0 * math.pi / size * turns.astype(jnp.float32)
    norm = 1.0 / math.sqrt(size)
    return (jnp.cos(angle) * norm, -jnp.sin(angle) * norm)


def chirp_phase(index, size):
    centred = index - size // 2
    period = 2 * fresnel_scale * size
    phase = centred * centred % period
    angle = math.pi / (fresnel_scale * size) * phase.astype(jnp.float32)
    return (jnp.cos(angle), jnp.sin(angle))


def contract(form, left_side, right_side):
    return jnp.einsum(
        form,
        left_side,
        right_side,
        precision=lax.Precision.HIGHEST,
        preferred_element_type=jnp.float32,
    )


def complex_mix(form, left_re, left_im, right_re, right_im):
    real_part = contract(form, left_re, right_re) - contract(form, left_im, right_im)
    imag_part = contract(form, left_re, right_im) + contract(form, left_im, right_re)
    return (real_part, imag_part)


def on_device(object_slice, probe_field, offsets, assignment, intensities):
    depth_count = lax.axis_size("depth")
    depth_index = lax.axis_index("depth")
    scan_count = lax.axis_size("scan")
    cycles = object_slice.shape[1]
    rows_dev = object_slice.shape[2]
    patch_side = probe_field.shape[2]
    pos_count = assignment.shape[0]
    total_pos = pos_count * scan_count
    width = object_slice.shape[3]
    full_width = scan_count * width
    all_slots = gather_blocks(assignment, "scan").reshape(total_pos)
    every_top = offsets[all_slots, 0]
    position = offsets[assignment]
    top_row = position[:, 0]
    left_col = position[:, 1]
    table_re, table_im = dft_table(patch_side)
    twice_re = jnp.concatenate([table_re, table_re], 0)
    twice_im = jnp.concatenate([table_im, table_im], 0)
    probe_twice = jnp.concatenate([probe_field, probe_field], 1)
    row_ids = jnp.arange(rows_dev, dtype=jnp.int32)
    col_ids = jnp.arange(patch_side, dtype=jnp.int32)
    col_cos, col_sin = chirp_phase(col_ids, patch_side)
    local_rows = depth_index * rows_dev + row_ids
    every_cycle = (every_top[:, None] + (local_rows[None, :] - every_top[:, None]) % patch_side) // patch_side
    gathered = gather_blocks(object_slice, "scan")
    full_band = jnp.moveaxis(gathered, 0, 3).reshape(object_slice.shape[:3] + (full_width,))
    shift_of = (local_rows[None, :] - top_row[:, None]) % patch_side
    cycle_of = (top_row[:, None] + shift_of) // patch_side
    obj_list, probe_list, t_re_list, t_im_list = [], [], [], []
    for slot in range(pos_count):
        chosen = full_band[:, 0]
        for cyc in range(1, cycles):
            chosen = jnp.where((cycle_of[slot] == cyc)[None, :, None], full_band[:, cyc], chosen)
        obj_list.append(lax.dynamic_slice_in_dim(chosen, left_col[slot], patch_side, 2))
        first_row = (depth_index * rows_dev - top_row[slot]) % patch_side
        probe_list.append(lax.dynamic_slice_in_dim(probe_twice, first_row, rows_dev, 1))
        table_start = (patch_side - top_row[slot] % patch_side) % patch_side
        t_re_list.append(lax.dynamic_slice_in_dim(twice_re, table_start, patch_side, 0))
        t_im_list.append(lax.dynamic_slice_in_dim(twice_im, table_start, patch_side, 0))
    patch = jnp.stack(obj_list)
    in_block = top_row % patch_side % rows_dev
    block_shift = top_row % patch_side // rows_dev
    patch_twice = jnp.concatenate([patch, patch], 2)
    rolled = jax.vmap(lambda t, b: lax.dynamic_slice_in_dim(t, b, rows_dev, 1))(patch_twice, in_block)
    upper = (row_ids[None, :] >= rows_dev - in_block[:, None])[:, None, :, None]
    aligned = jnp.where(upper, from_behind(rolled, "depth", depth_count - 1), rolled)
    levels = depth_count.bit_length() - 1
    for level in range(levels):
        moved = from_behind(aligned, "depth", depth_count - (1 << level))
        taken = (block_shift >> level & 1) == 1
        aligned = jnp.where(taken[:, None, None, None], moved, aligned)
    probe_rows = jnp.stack(probe_list)
    shift_re = jnp.stack(t_re_list)
    shift_im = jnp.stack(t_im_list)
    row_cos, row_sin = chirp_phase(shift_of, patch_side)
    chirp_re = (
        row_cos[:, :, None] * col_cos[None, None, :] - row_sin[:, :, None] * col_sin[None, None, :]
    )
    chirp_im = (
        row_sin[:, :, None] * col_cos[None, None, :] + row_cos[:, :, None] * col_sin[None, None, :]
    )
    obj_re = patch[:, 0].astype(jnp.float32)
    obj_im = patch[:, 1].astype(jnp.float32)
    probe_re = probe_rows[:, 0].astype(jnp.float32)
    probe_im = probe_rows[:, 1].astype(jnp.float32)
    wave_re = probe_re * obj_re - probe_im * obj_im
    wave_im = probe_re * obj_im + probe_im * obj_re
    psi_re = wave_re * chirp_re - wave_im * chirp_im
    psi_im = wave_re * chirp_im + wave_im * chirp_re
    half_re, half_im = complex_mix("vk,pjk->pvj", table_re, table_im, psi_re, psi_im)
    half_re, half_im = lax.all_to_all(
        jnp.stack([half_re, half_im]), "depth", split_axis=2, concat_axis=3, tiled=True
    )
    far_re, far_im = complex_mix("pvj,pju->pvu", half_re, half_im, shift_re, shift_im)
    excess = far_re * far_re + far_im * far_im - intensities
    resid_re = excess * far_re
    resid_im = excess * far_im
    mid_re, mid_im = complex_mix("pvu,pju->pvj", resid_re, resid_im, shift_re, -shift_im)
    mid_pair = jnp.stack([mid_re, mid_im], 1)
    mid_pair_twice = jnp.concatenate([mid_pair, mid_pair], 3)
    mid_probe = jax.vmap(lambda t, b: lax.dynamic_slice_in_dim(t, b, patch_side, 2))(
        mid_pair_twice, top_row % patch_side
    )
    mid_all = lax.all_to_all(
        jnp.stack([mid_pair, mid_probe]), "depth", split_axis=4, concat_axis=3, tiled=True
    )
    back_re, back_im = complex_mix(
        "vk,pvj->pjk", table_re, -table_im, mid_all[0, :, 0], mid_all[0, :, 1]
    )
    pback_re, pback_im = complex_mix(
        "vk,pvj->pjk", table_re, -table_im, mid_all[1, :, 0], mid_all[1, :, 1]
    )
    prow_cos, prow_sin = chirp_phase(local_rows, patch_side)
    pchirp_re = prow_cos[:, None] * col_cos[None, :] - prow_sin[:, None] * col_sin[None, :]
    pchirp_im = prow_sin[:, None] * col_cos[None, :] + prow_cos[:, None] * col_sin[None, :]
    pgrad_re = pback_re * pchirp_re + pback_im * pchirp_im
    pgrad_im = pback_im * pchirp_re - pback_re * pchirp_im
    win_re = aligned[:, 0].astype(jnp.float32)
    win_im = aligned[:, 1].astype(jnp.float32)
    grad_re = back_re * chirp_re + back_im * chirp_im
    grad_im = back_im * chirp_re - back_re * chirp_im
    contrib = jnp.stack(
        [probe_re * grad_re + probe_im * grad_im, probe_re * grad_im - probe_im * grad_re], 1
    )
    term = jnp.stack(
        [win_re * pgrad_re + win_im * pgrad_im, win_re * pgrad_im - win_im * pgrad_re], 1
    )
    placed = jnp.stack(
        [
            lax.dynamic_update_slice_in_dim(
                jnp.zeros((2, rows_dev, full_width), jnp.float32), contrib[slot], left_col[slot], 2
            )
            for slot in range(pos_count)
        ]
    )
    grad_chunks = jnp.moveaxis(placed.reshape(pos_count, 2, rows_dev, scan_count, width), 3, 0)
    probe_sum = jnp.sum(term, 0)
    grad_flat = grad_chunks.reshape(scan_count, -1)
    probe_flat = probe_sum.reshape(scan_count, -1)
    both_back = lax.all_to_all(
        jnp.concatenate([probe_flat, grad_flat], 1), "scan", 0, 0, tiled=True
    )
    probe_part = jnp.sum(both_back[:, : probe_flat.shape[1]], 0)
    grad_back = both_back[:, probe_flat.shape[1] :].reshape((total_pos, 2, rows_dev, width))
    object_grad = jnp.stack(
        [
            jnp.sum(jnp.where((every_cycle == cyc)[:, None, :, None], grad_back, 0.0), 0)
            for cyc in range(cycles)
        ],
        1,
    )
    probe_grad = gather_blocks(probe_part, "scan").reshape(probe_sum.shape)
    return (object_grad, probe_grad * total_pos ** (-0.5))


def solution(mesh):
    return jax.shard_map(
        on_device,
        mesh=mesh,
        in_specs=(P(None, None, "depth", "scan"), P(), P(), P("scan"), P("scan", "depth", None)),
        out_specs=(P(None, None, "depth", "scan"), P(None, "depth", None)),
        check_vma=False,
    )
```

```python
import math

import jax
import jax.numpy as jnp
from jax import lax
from jax.sharding import PartitionSpec as P

fresnel_scale = 4


def from_behind(block, axis, distance):
    devices = range(lax.axis_size(axis))
    route = [((i - distance) % len(devices), i) for i in devices]
    return lax.ppermute(block, axis, route)


def gather_blocks(block, axis):
    count = lax.axis_size(axis)
    spread = jnp.broadcast_to(block[None], (count,) + block.shape)
    return lax.all_to_all(spread, axis, 0, 0, tiled=True)


def sum_blocks(chunks, axis):
    return jnp.sum(lax.all_to_all(chunks, axis, 0, 0, tiled=True), 0)


def dft_table(size):
    index = jnp.arange(size, dtype=jnp.int32)
    turns = index[:, None] * index[None, :] % size
    angle = 2.0 * math.pi / size * turns.astype(jnp.float32)
    norm = 1.0 / math.sqrt(size)
    return (jnp.cos(angle) * norm, -jnp.sin(angle) * norm)


def chirp_phase(index, size):
    centred = index - size // 2
    period = 2 * fresnel_scale * size
    phase = centred * centred % period
    angle = math.pi / (fresnel_scale * size) * phase.astype(jnp.float32)
    return (jnp.cos(angle), jnp.sin(angle))


def contract(form, left_side, right_side):
    return jnp.einsum(
        form,
        left_side,
        right_side,
        precision=lax.Precision.HIGH,
        preferred_element_type=jnp.float32,
    )


def complex_mix(form, left_re, left_im, right_re, right_im):
    real_part = contract(form, left_re, right_re) - contract(form, left_im, right_im)
    imag_part = contract(form, left_re, right_im) + contract(form, left_im, right_re)
    return (real_part, imag_part)


def on_device(object_slice, probe_field, offsets, assignment, intensities):
    depth_count = lax.axis_size("depth")
    depth_index = lax.axis_index("depth")
    scan_count = lax.axis_size("scan")
    cycles = object_slice.shape[1]
    rows_dev = object_slice.shape[2]
    patch_side = probe_field.shape[2]
    pos_count = assignment.shape[0]
    total_pos = pos_count * scan_count
    width = object_slice.shape[3]
    full_width = scan_count * width
    all_slots = gather_blocks(assignment, "scan").reshape(total_pos)
    every_top = offsets[all_slots, 0]
    position = offsets[assignment]
    top_row = position[:, 0]
    left_col = position[:, 1]
    table_re, table_im = dft_table(patch_side)
    twice_re = jnp.concatenate([table_re, table_re], 0)
    twice_im = jnp.concatenate([table_im, table_im], 0)
    probe_twice = jnp.concatenate([probe_field, probe_field], 1)
    row_ids = jnp.arange(rows_dev, dtype=jnp.int32)
    col_ids = jnp.arange(patch_side, dtype=jnp.int32)
    col_cos, col_sin = chirp_phase(col_ids, patch_side)
    local_rows = depth_index * rows_dev + row_ids
    every_cycle = (every_top[:, None] + (local_rows[None, :] - every_top[:, None]) % patch_side) // patch_side
    gathered = gather_blocks(object_slice, "scan")
    full_band = jnp.moveaxis(gathered, 0, 3).reshape(object_slice.shape[:3] + (full_width,))
    shift_of = (local_rows[None, :] - top_row[:, None]) % patch_side
    cycle_of = (top_row[:, None] + shift_of) // patch_side
    obj_list, probe_list, t_re_list, t_im_list = [], [], [], []
    for slot in range(pos_count):
        chosen = full_band[:, 0]
        for cyc in range(1, cycles):
            chosen = jnp.where((cycle_of[slot] == cyc)[None, :, None], full_band[:, cyc], chosen)
        obj_list.append(lax.dynamic_slice_in_dim(chosen, left_col[slot], patch_side, 2))
        first_row = (depth_index * rows_dev - top_row[slot]) % patch_side
        probe_list.append(lax.dynamic_slice_in_dim(probe_twice, first_row, rows_dev, 1))
        table_start = (patch_side - top_row[slot] % patch_side) % patch_side
        t_re_list.append(lax.dynamic_slice_in_dim(twice_re, table_start, patch_side, 0))
        t_im_list.append(lax.dynamic_slice_in_dim(twice_im, table_start, patch_side, 0))
    patch = jnp.stack(obj_list)
    in_block = top_row % patch_side % rows_dev
    block_shift = top_row % patch_side // rows_dev
    patch_twice = jnp.concatenate([patch, patch], 2)
    rolled = jax.vmap(lambda t, b: lax.dynamic_slice_in_dim(t, b, rows_dev, 1))(patch_twice, in_block)
    upper = (row_ids[None, :] >= rows_dev - in_block[:, None])[:, None, :, None]
    aligned = jnp.where(upper, from_behind(rolled, "depth", depth_count - 1), rolled)
    levels = depth_count.bit_length() - 1
    for level in range(levels):
        moved = from_behind(aligned, "depth", depth_count - (1 << level))
        taken = (block_shift >> level & 1) == 1
        aligned = jnp.where(taken[:, None, None, None], moved, aligned)
    probe_rows = jnp.stack(probe_list)
    shift_re = jnp.stack(t_re_list)
    shift_im = jnp.stack(t_im_list)
    row_cos, row_sin = chirp_phase(shift_of, patch_side)
    chirp_re = (
        row_cos[:, :, None] * col_cos[None, None, :] - row_sin[:, :, None] * col_sin[None, None, :]
    )
    chirp_im = (
        row_sin[:, :, None] * col_cos[None, None, :] + row_cos[:, :, None] * col_sin[None, None, :]
    )
    obj_re = patch[:, 0].astype(jnp.float32)
    obj_im = patch[:, 1].astype(jnp.float32)
    probe_re = probe_rows[:, 0].astype(jnp.float32)
    probe_im = probe_rows[:, 1].astype(jnp.float32)
    wave_re = probe_re * obj_re - probe_im * obj_im
    wave_im = probe_re * obj_im + probe_im * obj_re
    psi_re = wave_re * chirp_re - wave_im * chirp_im
    psi_im = wave_re * chirp_im + wave_im * chirp_re
    half_re, half_im = complex_mix("vk,pjk->pvj", table_re, table_im, psi_re, psi_im)
    half_re, half_im = lax.all_to_all(
        jnp.stack([half_re, half_im]), "depth", split_axis=2, concat_axis=3, tiled=True
    )
    far_re, far_im = complex_mix("pvj,pju->pvu", half_re, half_im, shift_re, shift_im)
    excess = far_re * far_re + far_im * far_im - intensities
    resid_re = excess * far_re
    resid_im = excess * far_im
    mid_re, mid_im = complex_mix("pvu,pju->pvj", resid_re, resid_im, shift_re, -shift_im)
    mid_pair = jnp.stack([mid_re, mid_im], 1)
    mid_pair_twice = jnp.concatenate([mid_pair, mid_pair], 3)
    mid_probe = jax.vmap(lambda t, b: lax.dynamic_slice_in_dim(t, b, patch_side, 2))(
        mid_pair_twice, top_row % patch_side
    )
    mid_all = lax.all_to_all(
        jnp.stack([mid_pair, mid_probe]), "depth", split_axis=4, concat_axis=3, tiled=True
    )
    back_re, back_im = complex_mix(
        "vk,pvj->pjk", table_re, -table_im, mid_all[0, :, 0], mid_all[0, :, 1]
    )
    pback_re, pback_im = complex_mix(
        "vk,pvj->pjk", table_re, -table_im, mid_all[1, :, 0], mid_all[1, :, 1]
    )
    prow_cos, prow_sin = chirp_phase(local_rows, patch_side)
    pchirp_re = prow_cos[:, None] * col_cos[None, :] - prow_sin[:, None] * col_sin[None, :]
    pchirp_im = prow_sin[:, None] * col_cos[None, :] + prow_cos[:, None] * col_sin[None, :]
    pgrad_re = pback_re * pchirp_re + pback_im * pchirp_im
    pgrad_im = pback_im * pchirp_re - pback_re * pchirp_im
    win_re = aligned[:, 0].astype(jnp.float32)
    win_im = aligned[:, 1].astype(jnp.float32)
    grad_re = back_re * chirp_re + back_im * chirp_im
    grad_im = back_im * chirp_re - back_re * chirp_im
    contrib = jnp.stack(
        [probe_re * grad_re + probe_im * grad_im, probe_re * grad_im - probe_im * grad_re], 1
    )
    term = jnp.stack(
        [win_re * pgrad_re + win_im * pgrad_im, win_re * pgrad_im - win_im * pgrad_re], 1
    )
    placed = jnp.stack(
        [
            lax.dynamic_update_slice_in_dim(
                jnp.zeros((2, rows_dev, full_width), jnp.float32), contrib[slot], left_col[slot], 2
            )
            for slot in range(pos_count)
        ]
    )
    grad_chunks = jnp.moveaxis(placed.reshape(pos_count, 2, rows_dev, scan_count, width), 3, 0)
    probe_sum = jnp.sum(term, 0)
    grad_flat = grad_chunks.reshape(scan_count, -1)
    probe_flat = probe_sum.reshape(scan_count, -1)
    both_back = lax.all_to_all(
        jnp.concatenate([probe_flat, grad_flat], 1), "scan", 0, 0, tiled=True
    )
    probe_part = jnp.sum(both_back[:, : probe_flat.shape[1]], 0)
    grad_back = both_back[:, probe_flat.shape[1] :].reshape((total_pos, 2, rows_dev, width))
    object_grad = jnp.stack(
        [
            jnp.sum(jnp.where((every_cycle == cyc)[:, None, :, None], grad_back, 0.0), 0)
            for cyc in range(cycles)
        ],
        1,
    )
    probe_grad = gather_blocks(probe_part, "scan").reshape(probe_sum.shape)
    return (object_grad, probe_grad * total_pos ** (-0.5))


def solution(mesh):
    return jax.shard_map(
        on_device,
        mesh=mesh,
        in_specs=(P(None, None, "depth", "scan"), P(), P(), P("scan"), P("scan", "depth", None)),
        out_specs=(P(None, None, "depth", "scan"), P(None, "depth", None)),
        check_vma=False,
    )
```

```python
import math

import jax
import jax.numpy as jnp
from jax import lax
from jax.sharding import PartitionSpec as P

fresnel_scale = 4


def from_behind(block, axis, distance):
    devices = range(lax.axis_size(axis))
    route = [((i - distance) % len(devices), i) for i in devices]
    return lax.ppermute(block, axis, route)


def gather_blocks(block, axis):
    count = lax.axis_size(axis)
    spread = jnp.broadcast_to(block[None], (count,) + block.shape)
    return lax.all_to_all(spread, axis, 0, 0, tiled=True)


def sum_blocks(chunks, axis):
    return jnp.sum(lax.all_to_all(chunks, axis, 0, 0, tiled=True), 0)


def dft_table(size):
    index = jnp.arange(size, dtype=jnp.int32)
    turns = index[:, None] * index[None, :] % size
    angle = 2.0 * math.pi / size * turns.astype(jnp.float32)
    norm = 1.0 / math.sqrt(size)
    return (jnp.cos(angle) * norm, -jnp.sin(angle) * norm)


def chirp_phase(index, size):
    centred = index - size // 2
    period = 2 * fresnel_scale * size
    phase = centred * centred % period
    angle = math.pi / (fresnel_scale * size) * phase.astype(jnp.float32)
    return (jnp.cos(angle), jnp.sin(angle))


def contract(form, left_side, right_side):
    return jnp.einsum(
        form,
        left_side,
        right_side,
        precision=lax.Precision.HIGHEST,
        preferred_element_type=jnp.float32,
    )


def complex_mix(form, left_re, left_im, right_re, right_im):
    real_part = contract(form, left_re, right_re) - contract(form, left_im, right_im)
    imag_part = contract(form, left_re, right_im) + contract(form, left_im, right_re)
    return (real_part, imag_part)


def on_device(object_slice, probe_field, offsets, assignment, intensities):
    depth_count = lax.axis_size("depth")
    depth_index = lax.axis_index("depth")
    scan_count = lax.axis_size("scan")
    cycles = object_slice.shape[1]
    rows_dev = object_slice.shape[2]
    patch_side = probe_field.shape[2]
    pos_count = assignment.shape[0]
    total_pos = pos_count * scan_count
    width = object_slice.shape[3]
    full_width = scan_count * width
    all_slots = gather_blocks(assignment, "scan").reshape(total_pos)
    every_top = offsets[all_slots, 0]
    position = offsets[assignment]
    top_row = position[:, 0]
    left_col = position[:, 1]
    table_re, table_im = dft_table(patch_side)
    twice_re = jnp.concatenate([table_re, table_re], 0)
    twice_im = jnp.concatenate([table_im, table_im], 0)
    probe_twice = jnp.concatenate([probe_field, probe_field], 1)
    row_ids = jnp.arange(rows_dev, dtype=jnp.int32)
    col_ids = jnp.arange(patch_side, dtype=jnp.int32)
    col_cos, col_sin = chirp_phase(col_ids, patch_side)
    local_rows = depth_index * rows_dev + row_ids
    every_cycle = (every_top[:, None] + (local_rows[None, :] - every_top[:, None]) % patch_side) // patch_side
    gathered = gather_blocks(object_slice, "scan")
    full_band = jnp.moveaxis(gathered, 0, 3).reshape(object_slice.shape[:3] + (full_width,))
    shift_of = (local_rows[None, :] - top_row[:, None]) % patch_side
    cycle_of = (top_row[:, None] + shift_of) // patch_side
    obj_list, probe_list, t_re_list, t_im_list = [], [], [], []
    for slot in range(pos_count):
        chosen = full_band[:, 0]
        for cyc in range(1, cycles):
            chosen = jnp.where((cycle_of[slot] == cyc)[None, :, None], full_band[:, cyc], chosen)
        obj_list.append(lax.dynamic_slice_in_dim(chosen, left_col[slot], patch_side, 2))
        first_row = (depth_index * rows_dev - top_row[slot]) % patch_side
        probe_list.append(lax.dynamic_slice_in_dim(probe_twice, first_row, rows_dev, 1))
        table_start = (patch_side - top_row[slot] % patch_side) % patch_side
        t_re_list.append(lax.dynamic_slice_in_dim(twice_re, table_start, patch_side, 0))
        t_im_list.append(lax.dynamic_slice_in_dim(twice_im, table_start, patch_side, 0))
    patch = jnp.stack(obj_list)
    in_block = top_row % patch_side % rows_dev
    block_shift = top_row % patch_side // rows_dev
    patch_twice = jnp.concatenate([patch, patch], 2)
    rolled = jax.vmap(lambda t, b: lax.dynamic_slice_in_dim(t, b, rows_dev, 1))(patch_twice, in_block)
    upper = (row_ids[None, :] >= rows_dev - in_block[:, None])[:, None, :, None]
    aligned = jnp.where(upper, from_behind(rolled, "depth", depth_count - 1), rolled)
    levels = depth_count.bit_length() - 1
    for level in range(levels):
        moved = from_behind(aligned, "depth", depth_count - (1 << level))
        taken = (block_shift >> level & 1) == 1
        aligned = jnp.where(taken[:, None, None, None], moved, aligned)
    probe_rows = jnp.stack(probe_list)
    shift_re = jnp.stack(t_re_list)
    shift_im = jnp.stack(t_im_list)
    row_cos, row_sin = chirp_phase(shift_of, patch_side)
    chirp_re = (
        row_cos[:, :, None] * col_cos[None, None, :] - row_sin[:, :, None] * col_sin[None, None, :]
    )
    chirp_im = (
        row_sin[:, :, None] * col_cos[None, None, :] + row_cos[:, :, None] * col_sin[None, None, :]
    )
    obj_re = patch[:, 0].astype(jnp.float32)
    obj_im = patch[:, 1].astype(jnp.float32)
    probe_re = probe_rows[:, 0].astype(jnp.float32)
    probe_im = probe_rows[:, 1].astype(jnp.float32)
    wave_re = probe_re * obj_re - probe_im * obj_im
    wave_im = probe_re * obj_im + probe_im * obj_re
    psi_re = wave_re * chirp_re - wave_im * chirp_im
    psi_im = wave_re * chirp_im + wave_im * chirp_re
    half_re, half_im = complex_mix("pjk,kv->pvj", psi_re, psi_im, table_re, table_im)
    half_re, half_im = lax.all_to_all(
        jnp.stack([half_re, half_im]), "depth", split_axis=2, concat_axis=3, tiled=True
    )
    far_re, far_im = complex_mix("pvj,pju->pvu", half_re, half_im, shift_re, shift_im)
    excess = far_re * far_re + far_im * far_im - intensities
    resid_re = excess * far_re
    resid_im = excess * far_im
    mid_re, mid_im = complex_mix("pvu,pju->pvj", resid_re, resid_im, shift_re, -shift_im)
    mid_pair = jnp.stack([mid_re, mid_im], 1)
    mid_pair_twice = jnp.concatenate([mid_pair, mid_pair], 3)
    mid_probe = jax.vmap(lambda t, b: lax.dynamic_slice_in_dim(t, b, patch_side, 2))(
        mid_pair_twice, top_row % patch_side
    )
    mid_all = lax.all_to_all(
        jnp.stack([mid_pair, mid_probe]), "depth", split_axis=4, concat_axis=3, tiled=True
    )
    mid_rows = jnp.swapaxes(mid_all, 3, 4)
    back_re, back_im = complex_mix(
        "pjv,vk->pjk", mid_rows[0, :, 0], mid_rows[0, :, 1], table_re, -table_im
    )
    pback_re, pback_im = complex_mix(
        "pjv,vk->pjk", mid_rows[1, :, 0], mid_rows[1, :, 1], table_re, -table_im
    )
    prow_cos, prow_sin = chirp_phase(local_rows, patch_side)
    pchirp_re = prow_cos[:, None] * col_cos[None, :] - prow_sin[:, None] * col_sin[None, :]
    pchirp_im = prow_sin[:, None] * col_cos[None, :] + prow_cos[:, None] * col_sin[None, :]
    pgrad_re = pback_re * pchirp_re + pback_im * pchirp_im
    pgrad_im = pback_im * pchirp_re - pback_re * pchirp_im
    win_re = aligned[:, 0].astype(jnp.float32)
    win_im = aligned[:, 1].astype(jnp.float32)
    grad_re = back_re * chirp_re + back_im * chirp_im
    grad_im = back_im * chirp_re - back_re * chirp_im
    contrib = jnp.stack(
        [probe_re * grad_re + probe_im * grad_im, probe_re * grad_im - probe_im * grad_re], 1
    )
    term = jnp.stack(
        [win_re * pgrad_re + win_im * pgrad_im, win_re * pgrad_im - win_im * pgrad_re], 1
    )
    placed = jnp.stack(
        [
            lax.dynamic_update_slice_in_dim(
                jnp.zeros((2, rows_dev, full_width), jnp.float32), contrib[slot], left_col[slot], 2
            )
            for slot in range(pos_count)
        ]
    )
    grad_chunks = jnp.moveaxis(placed.reshape(pos_count, 2, rows_dev, scan_count, width), 3, 0)
    probe_sum = jnp.sum(term, 0)
    grad_flat = grad_chunks.reshape(scan_count, -1)
    probe_flat = probe_sum.reshape(scan_count, -1)
    both_back = lax.all_to_all(
        jnp.concatenate([probe_flat, grad_flat], 1), "scan", 0, 0, tiled=True
    )
    probe_part = jnp.sum(both_back[:, : probe_flat.shape[1]], 0)
    grad_back = both_back[:, probe_flat.shape[1] :].reshape((total_pos, 2, rows_dev, width))
    object_grad = jnp.stack(
        [
            jnp.sum(jnp.where((every_cycle == cyc)[:, None, :, None], grad_back, 0.0), 0)
            for cyc in range(cycles)
        ],
        1,
    )
    probe_grad = gather_blocks(probe_part, "scan").reshape(probe_sum.shape)
    return (object_grad, probe_grad * total_pos ** (-0.5))


def solution(mesh):
    return jax.shard_map(
        on_device,
        mesh=mesh,
        in_specs=(P(None, None, "depth", "scan"), P(), P(), P("scan"), P("scan", "depth", None)),
        out_specs=(P(None, None, "depth", "scan"), P(None, "depth", None)),
        check_vma=False,
    )
```

```python
import math

import jax
import jax.numpy as jnp
from jax import lax
from jax.sharding import PartitionSpec as P

fresnel_scale = 4


def from_behind(block, axis, distance):
    devices = range(lax.axis_size(axis))
    route = [((i - distance) % len(devices), i) for i in devices]
    return lax.ppermute(block, axis, route)


def gather_blocks(block, axis):
    count = lax.axis_size(axis)
    spread = jnp.broadcast_to(block[None], (count,) + block.shape)
    return lax.all_to_all(spread, axis, 0, 0, tiled=True)


def sum_blocks(chunks, axis):
    return jnp.sum(lax.all_to_all(chunks, axis, 0, 0, tiled=True), 0)


def dft_table(size):
    index = jnp.arange(size, dtype=jnp.int32)
    turns = index[:, None] * index[None, :] % size
    angle = 2.0 * math.pi / size * turns.astype(jnp.float32)
    norm = 1.0 / math.sqrt(size)
    return (jnp.cos(angle) * norm, -jnp.sin(angle) * norm)


def chirp_phase(index, size):
    centred = index - size // 2
    period = 2 * fresnel_scale * size
    phase = centred * centred % period
    angle = math.pi / (fresnel_scale * size) * phase.astype(jnp.float32)
    return (jnp.cos(angle), jnp.sin(angle))


def contract(form, left_side, right_side, precision=lax.Precision.HIGHEST):
    return jnp.einsum(
        form,
        left_side,
        right_side,
        precision=precision,
        preferred_element_type=jnp.float32,
    )


def complex_mix(form, left_re, left_im, right_re, right_im, precision=lax.Precision.HIGHEST):
    real_part = contract(form, left_re, right_re, precision) - contract(
        form, left_im, right_im, precision
    )
    imag_part = contract(form, left_re, right_im, precision) + contract(
        form, left_im, right_re, precision
    )
    return (real_part, imag_part)


def on_device(object_slice, probe_field, offsets, assignment, intensities):
    depth_count = lax.axis_size("depth")
    depth_index = lax.axis_index("depth")
    scan_count = lax.axis_size("scan")
    cycles = object_slice.shape[1]
    rows_dev = object_slice.shape[2]
    patch_side = probe_field.shape[2]
    pos_count = assignment.shape[0]
    total_pos = pos_count * scan_count
    width = object_slice.shape[3]
    full_width = scan_count * width
    all_slots = gather_blocks(assignment, "scan").reshape(total_pos)
    every_top = offsets[all_slots, 0]
    position = offsets[assignment]
    top_row = position[:, 0]
    left_col = position[:, 1]
    table_re, table_im = dft_table(patch_side)
    twice_re = jnp.concatenate([table_re, table_re], 0)
    twice_im = jnp.concatenate([table_im, table_im], 0)
    probe_twice = jnp.concatenate([probe_field, probe_field], 1)
    row_ids = jnp.arange(rows_dev, dtype=jnp.int32)
    col_ids = jnp.arange(patch_side, dtype=jnp.int32)
    col_cos, col_sin = chirp_phase(col_ids, patch_side)
    local_rows = depth_index * rows_dev + row_ids
    every_cycle = (every_top[:, None] + (local_rows[None, :] - every_top[:, None]) % patch_side) // patch_side
    gathered = gather_blocks(object_slice, "scan")
    full_band = jnp.moveaxis(gathered, 0, 3).reshape(object_slice.shape[:3] + (full_width,))
    shift_of = (local_rows[None, :] - top_row[:, None]) % patch_side
    cycle_of = (top_row[:, None] + shift_of) // patch_side
    obj_list, probe_list, t_re_list, t_im_list = [], [], [], []
    for slot in range(pos_count):
        chosen = full_band[:, 0]
        for cyc in range(1, cycles):
            chosen = jnp.where((cycle_of[slot] == cyc)[None, :, None], full_band[:, cyc], chosen)
        obj_list.append(lax.dynamic_slice_in_dim(chosen, left_col[slot], patch_side, 2))
        first_row = (depth_index * rows_dev - top_row[slot]) % patch_side
        probe_list.append(lax.dynamic_slice_in_dim(probe_twice, first_row, rows_dev, 1))
        table_start = (patch_side - top_row[slot] % patch_side) % patch_side
        t_re_list.append(lax.dynamic_slice_in_dim(twice_re, table_start, patch_side, 0))
        t_im_list.append(lax.dynamic_slice_in_dim(twice_im, table_start, patch_side, 0))
    patch = jnp.stack(obj_list)
    in_block = top_row % patch_side % rows_dev
    block_shift = top_row % patch_side // rows_dev
    patch_twice = jnp.concatenate([patch, patch], 2)
    rolled = jax.vmap(lambda t, b: lax.dynamic_slice_in_dim(t, b, rows_dev, 1))(patch_twice, in_block)
    upper = (row_ids[None, :] >= rows_dev - in_block[:, None])[:, None, :, None]
    aligned = jnp.where(upper, from_behind(rolled, "depth", depth_count - 1), rolled)
    levels = depth_count.bit_length() - 1
    for level in range(levels):
        moved = from_behind(aligned, "depth", depth_count - (1 << level))
        taken = (block_shift >> level & 1) == 1
        aligned = jnp.where(taken[:, None, None, None], moved, aligned)
    probe_rows = jnp.stack(probe_list)
    shift_re = jnp.stack(t_re_list)
    shift_im = jnp.stack(t_im_list)
    row_cos, row_sin = chirp_phase(shift_of, patch_side)
    chirp_re = (
        row_cos[:, :, None] * col_cos[None, None, :] - row_sin[:, :, None] * col_sin[None, None, :]
    )
    chirp_im = (
        row_sin[:, :, None] * col_cos[None, None, :] + row_cos[:, :, None] * col_sin[None, None, :]
    )
    obj_re = patch[:, 0].astype(jnp.float32)
    obj_im = patch[:, 1].astype(jnp.float32)
    probe_re = probe_rows[:, 0].astype(jnp.float32)
    probe_im = probe_rows[:, 1].astype(jnp.float32)
    wave_re = probe_re * obj_re - probe_im * obj_im
    wave_im = probe_re * obj_im + probe_im * obj_re
    psi_re = wave_re * chirp_re - wave_im * chirp_im
    psi_im = wave_re * chirp_im + wave_im * chirp_re
    half_re, half_im = complex_mix("pjk,kv->pvj", psi_re, psi_im, table_re, table_im)
    half_re, half_im = lax.all_to_all(
        jnp.stack([half_re, half_im]), "depth", split_axis=2, concat_axis=3, tiled=True
    )
    far_re, far_im = complex_mix("pvj,pju->pvu", half_re, half_im, shift_re, shift_im)
    excess = far_re * far_re + far_im * far_im - intensities
    resid_re = excess * far_re
    resid_im = excess * far_im
    mid_re, mid_im = complex_mix("pvu,pju->pvj", resid_re, resid_im, shift_re, -shift_im)
    mid_pair = jnp.stack([mid_re, mid_im], 1)
    mid_pair_twice = jnp.concatenate([mid_pair, mid_pair], 3)
    mid_probe = jax.vmap(lambda t, b: lax.dynamic_slice_in_dim(t, b, patch_side, 2))(
        mid_pair_twice, top_row % patch_side
    )
    mid_all = lax.all_to_all(
        jnp.stack([mid_pair, mid_probe]), "depth", split_axis=4, concat_axis=3, tiled=True
    )
    mid_rows = jnp.swapaxes(mid_all, 3, 4)
    back_re, back_im = complex_mix(
        "pjv,vk->pjk", mid_rows[0, :, 0], mid_rows[0, :, 1], table_re, -table_im, lax.Precision.HIGH
    )
    pback_re, pback_im = complex_mix(
        "pjv,vk->pjk", mid_rows[1, :, 0], mid_rows[1, :, 1], table_re, -table_im, lax.Precision.HIGH
    )
    prow_cos, prow_sin = chirp_phase(local_rows, patch_side)
    pchirp_re = prow_cos[:, None] * col_cos[None, :] - prow_sin[:, None] * col_sin[None, :]
    pchirp_im = prow_sin[:, None] * col_cos[None, :] + prow_cos[:, None] * col_sin[None, :]
    pgrad_re = pback_re * pchirp_re + pback_im * pchirp_im
    pgrad_im = pback_im * pchirp_re - pback_re * pchirp_im
    win_re = aligned[:, 0].astype(jnp.float32)
    win_im = aligned[:, 1].astype(jnp.float32)
    grad_re = back_re * chirp_re + back_im * chirp_im
    grad_im = back_im * chirp_re - back_re * chirp_im
    contrib = jnp.stack(
        [probe_re * grad_re + probe_im * grad_im, probe_re * grad_im - probe_im * grad_re], 1
    )
    term = jnp.stack(
        [win_re * pgrad_re + win_im * pgrad_im, win_re * pgrad_im - win_im * pgrad_re], 1
    )
    placed = jnp.stack(
        [
            lax.dynamic_update_slice_in_dim(
                jnp.zeros((2, rows_dev, full_width), jnp.float32), contrib[slot], left_col[slot], 2
            )
            for slot in range(pos_count)
        ]
    )
    grad_chunks = jnp.moveaxis(placed.reshape(pos_count, 2, rows_dev, scan_count, width), 3, 0)
    probe_sum = jnp.sum(term, 0)
    grad_flat = grad_chunks.reshape(scan_count, -1)
    probe_flat = probe_sum.reshape(scan_count, -1)
    both_back = lax.all_to_all(
        jnp.concatenate([probe_flat, grad_flat], 1), "scan", 0, 0, tiled=True
    )
    probe_part = jnp.sum(both_back[:, : probe_flat.shape[1]], 0)
    grad_back = both_back[:, probe_flat.shape[1] :].reshape((total_pos, 2, rows_dev, width))
    object_grad = jnp.stack(
        [
            jnp.sum(jnp.where((every_cycle == cyc)[:, None, :, None], grad_back, 0.0), 0)
            for cyc in range(cycles)
        ],
        1,
    )
    probe_grad = gather_blocks(probe_part, "scan").reshape(probe_sum.shape)
    return (object_grad, probe_grad * total_pos ** (-0.5))


def solution(mesh):
    return jax.shard_map(
        on_device,
        mesh=mesh,
        in_specs=(P(None, None, "depth", "scan"), P(), P(), P("scan"), P("scan", "depth", None)),
        out_specs=(P(None, None, "depth", "scan"), P(None, "depth", None)),
        check_vma=False,
    )
```

```python
import math

import jax
import jax.numpy as jnp
from jax import lax
from jax.sharding import PartitionSpec as P

fresnel_scale = 4


def from_behind(block, axis, distance):
    devices = range(lax.axis_size(axis))
    route = [((i - distance) % len(devices), i) for i in devices]
    return lax.ppermute(block, axis, route)


def gather_blocks(block, axis):
    count = lax.axis_size(axis)
    spread = jnp.broadcast_to(block[None], (count,) + block.shape)
    return lax.all_to_all(spread, axis, 0, 0, tiled=True)


def sum_blocks(chunks, axis):
    return jnp.sum(lax.all_to_all(chunks, axis, 0, 0, tiled=True), 0)


def dft_table(size):
    index = jnp.arange(size, dtype=jnp.int32)
    turns = index[:, None] * index[None, :] % size
    angle = 2.0 * math.pi / size * turns.astype(jnp.float32)
    norm = 1.0 / math.sqrt(size)
    return (jnp.cos(angle) * norm, -jnp.sin(angle) * norm)


def chirp_phase(index, size):
    centred = index - size // 2
    period = 2 * fresnel_scale * size
    phase = centred * centred % period
    angle = math.pi / (fresnel_scale * size) * phase.astype(jnp.float32)
    return (jnp.cos(angle), jnp.sin(angle))


def contract(form, left_side, right_side, precision=lax.Precision.HIGHEST):
    return jnp.einsum(
        form,
        left_side,
        right_side,
        precision=precision,
        preferred_element_type=jnp.float32,
    )


def complex_mix(form, left_re, left_im, right_re, right_im, precision=lax.Precision.HIGHEST):
    real_part = contract(form, left_re, right_re, precision) - contract(
        form, left_im, right_im, precision
    )
    imag_part = contract(form, left_re, right_im, precision) + contract(
        form, left_im, right_re, precision
    )
    return (real_part, imag_part)


def on_device(object_slice, probe_field, offsets, assignment, intensities):
    depth_count = lax.axis_size("depth")
    depth_index = lax.axis_index("depth")
    scan_count = lax.axis_size("scan")
    cycles = object_slice.shape[1]
    rows_dev = object_slice.shape[2]
    patch_side = probe_field.shape[2]
    pos_count = assignment.shape[0]
    total_pos = pos_count * scan_count
    width = object_slice.shape[3]
    full_width = scan_count * width
    position = offsets[assignment]
    top_row = position[:, 0]
    left_col = position[:, 1]
    top_code = jnp.concatenate([top_row // rows_dev, top_row % rows_dev]).astype(object_slice.dtype)
    block_size = object_slice.size
    carried = gather_blocks(jnp.concatenate([object_slice.reshape(-1), top_code]), "scan")
    tops = carried[:, block_size:].astype(jnp.int32)
    every_top = (tops[:, :pos_count] * rows_dev + tops[:, pos_count:]).reshape(total_pos)
    table_re, table_im = dft_table(patch_side)
    twice_re = jnp.concatenate([table_re, table_re], 0)
    twice_im = jnp.concatenate([table_im, table_im], 0)
    probe_twice = jnp.concatenate([probe_field, probe_field], 1)
    row_ids = jnp.arange(rows_dev, dtype=jnp.int32)
    col_ids = jnp.arange(patch_side, dtype=jnp.int32)
    col_cos, col_sin = chirp_phase(col_ids, patch_side)
    local_rows = depth_index * rows_dev + row_ids
    every_cycle = (every_top[:, None] + (local_rows[None, :] - every_top[:, None]) % patch_side) // patch_side
    gathered = carried[:, :block_size].reshape((scan_count,) + object_slice.shape)
    full_band = jnp.moveaxis(gathered, 0, 3).reshape(object_slice.shape[:3] + (full_width,))
    shift_of = (local_rows[None, :] - top_row[:, None]) % patch_side
    cycle_of = (top_row[:, None] + shift_of) // patch_side
    obj_list, probe_list, t_re_list, t_im_list = [], [], [], []
    for slot in range(pos_count):
        chosen = full_band[:, 0]
        for cyc in range(1, cycles):
            chosen = jnp.where((cycle_of[slot] == cyc)[None, :, None], full_band[:, cyc], chosen)
        obj_list.append(lax.dynamic_slice_in_dim(chosen, left_col[slot], patch_side, 2))
        first_row = (depth_index * rows_dev - top_row[slot]) % patch_side
        probe_list.append(lax.dynamic_slice_in_dim(probe_twice, first_row, rows_dev, 1))
        table_start = (patch_side - top_row[slot] % patch_side) % patch_side
        t_re_list.append(lax.dynamic_slice_in_dim(twice_re, table_start, patch_side, 0))
        t_im_list.append(lax.dynamic_slice_in_dim(twice_im, table_start, patch_side, 0))
    patch = jnp.stack(obj_list)
    in_block = top_row % patch_side % rows_dev
    block_shift = top_row % patch_side // rows_dev
    patch_twice = jnp.concatenate([patch, patch], 2)
    rolled = jax.vmap(lambda t, b: lax.dynamic_slice_in_dim(t, b, rows_dev, 1))(patch_twice, in_block)
    upper = (row_ids[None, :] >= rows_dev - in_block[:, None])[:, None, :, None]
    aligned = jnp.where(upper, from_behind(rolled, "depth", depth_count - 1), rolled)
    levels = depth_count.bit_length() - 1
    for level in range(levels):
        moved = from_behind(aligned, "depth", depth_count - (1 << level))
        taken = (block_shift >> level & 1) == 1
        aligned = jnp.where(taken[:, None, None, None], moved, aligned)
    probe_rows = jnp.stack(probe_list)
    shift_re = jnp.stack(t_re_list)
    shift_im = jnp.stack(t_im_list)
    row_cos, row_sin = chirp_phase(shift_of, patch_side)
    chirp_re = (
        row_cos[:, :, None] * col_cos[None, None, :] - row_sin[:, :, None] * col_sin[None, None, :]
    )
    chirp_im = (
        row_sin[:, :, None] * col_cos[None, None, :] + row_cos[:, :, None] * col_sin[None, None, :]
    )
    obj_re = patch[:, 0].astype(jnp.float32)
    obj_im = patch[:, 1].astype(jnp.float32)
    probe_re = probe_rows[:, 0].astype(jnp.float32)
    probe_im = probe_rows[:, 1].astype(jnp.float32)
    wave_re = probe_re * obj_re - probe_im * obj_im
    wave_im = probe_re * obj_im + probe_im * obj_re
    psi_re = wave_re * chirp_re - wave_im * chirp_im
    psi_im = wave_re * chirp_im + wave_im * chirp_re
    half_re, half_im = complex_mix("pjk,kv->pvj", psi_re, psi_im, table_re, table_im)
    half_re, half_im = lax.all_to_all(
        jnp.stack([half_re, half_im]), "depth", split_axis=2, concat_axis=3, tiled=True
    )
    far_re, far_im = complex_mix("pvj,pju->pvu", half_re, half_im, shift_re, shift_im)
    excess = far_re * far_re + far_im * far_im - intensities
    resid_re = excess * far_re
    resid_im = excess * far_im
    mid_re, mid_im = complex_mix("pvu,pju->pvj", resid_re, resid_im, shift_re, -shift_im)
    mid_pair = jnp.stack([mid_re, mid_im], 1)
    mid_pair_twice = jnp.concatenate([mid_pair, mid_pair], 3)
    mid_probe = jax.vmap(lambda t, b: lax.dynamic_slice_in_dim(t, b, patch_side, 2))(
        mid_pair_twice, top_row % patch_side
    )
    mid_all = lax.all_to_all(
        jnp.stack([mid_pair, mid_probe]), "depth", split_axis=4, concat_axis=3, tiled=True
    )
    mid_rows = jnp.swapaxes(mid_all, 3, 4)
    back_re, back_im = complex_mix(
        "pjv,vk->pjk", mid_rows[0, :, 0], mid_rows[0, :, 1], table_re, -table_im, lax.Precision.HIGH
    )
    pback_re, pback_im = complex_mix(
        "pjv,vk->pjk", mid_rows[1, :, 0], mid_rows[1, :, 1], table_re, -table_im, lax.Precision.HIGH
    )
    prow_cos, prow_sin = chirp_phase(local_rows, patch_side)
    pchirp_re = prow_cos[:, None] * col_cos[None, :] - prow_sin[:, None] * col_sin[None, :]
    pchirp_im = prow_sin[:, None] * col_cos[None, :] + prow_cos[:, None] * col_sin[None, :]
    pgrad_re = pback_re * pchirp_re + pback_im * pchirp_im
    pgrad_im = pback_im * pchirp_re - pback_re * pchirp_im
    win_re = aligned[:, 0].astype(jnp.float32)
    win_im = aligned[:, 1].astype(jnp.float32)
    grad_re = back_re * chirp_re + back_im * chirp_im
    grad_im = back_im * chirp_re - back_re * chirp_im
    contrib = jnp.stack(
        [probe_re * grad_re + probe_im * grad_im, probe_re * grad_im - probe_im * grad_re], 1
    )
    term = jnp.stack(
        [win_re * pgrad_re + win_im * pgrad_im, win_re * pgrad_im - win_im * pgrad_re], 1
    )
    placed = jnp.stack(
        [
            lax.dynamic_update_slice_in_dim(
                jnp.zeros((2, rows_dev, full_width), jnp.float32), contrib[slot], left_col[slot], 2
            )
            for slot in range(pos_count)
        ]
    )
    grad_chunks = jnp.moveaxis(placed.reshape(pos_count, 2, rows_dev, scan_count, width), 3, 0)
    probe_sum = jnp.sum(term, 0)
    grad_flat = grad_chunks.reshape(scan_count, -1)
    probe_flat = probe_sum.reshape(scan_count, -1)
    probe_part = sum_blocks(probe_flat, "scan")
    spread_part = jnp.broadcast_to(probe_part[None], probe_flat.shape)
    both_back = lax.all_to_all(
        jnp.concatenate([spread_part, grad_flat], 1), "scan", 0, 0, tiled=True
    )
    probe_grad = both_back[:, : probe_flat.shape[1]].reshape(probe_sum.shape)
    grad_back = both_back[:, probe_flat.shape[1] :].reshape((total_pos, 2, rows_dev, width))
    object_grad = jnp.stack(
        [
            jnp.sum(jnp.where((every_cycle == cyc)[:, None, :, None], grad_back, 0.0), 0)
            for cyc in range(cycles)
        ],
        1,
    )
    return (object_grad, probe_grad * total_pos ** (-0.5))


def solution(mesh):
    return jax.shard_map(
        on_device,
        mesh=mesh,
        in_specs=(P(None, None, "depth", "scan"), P(), P(), P("scan"), P("scan", "depth", None)),
        out_specs=(P(None, None, "depth", "scan"), P(None, "depth", None)),
        check_vma=False,
    )
```
